256 devices in a mesh: pipe: 4 (over x), expert: 64 (over z, y, core).
Axes of the slice: x: 4, y: 4, z: 8, core: 2. Of those that a mesh axis runs over, the one named last changes fastest.
Arguments:
- saved_inputs: bfloat16 [4, 3, 4096, 2048], P('pipe', None, 'expert'), may hold values from -6 to 6
- routes: int32 [4, 3, 4096, 4], P('pipe', None, 'expert'), may hold values from 0 to 63, as said below
- gates: float32 [4, 3, 4096, 4], P('pipe', None, 'expert'), may hold values from 0.1 to 0.6
- w_in: bfloat16 [4, 64, 2048, 768], P('pipe', 'expert'), may hold values from -0.125 to 0.125
- w_out: bfloat16 [4, 64, 768, 2048], P('pipe', 'expert'), may hold values from -0.21875 to 0.21875
- cotangent: bfloat16 [3, 4096, 2048], P(None, 'expert', 'pipe'), may hold values from -6 to 6
Outputs:
- grad_in: bfloat16 [3, 4096, 2048], P(None, 'expert', 'pipe')
- grad_w_in: bfloat16 [4, 64, 2048, 768], P('pipe', 'expert')
- grad_w_out: bfloat16 [4, 64, 768, 2048], P('pipe', 'expert')
The draws below stay inside these ranges and needn't reach their ends.
Inputs may be any that keep to these rules, and one draw needn't show every extreme that they name: `routes`: each token names 4 different experts. Among the 64 tokens of one device's micro-batch (aligned blocks of the token dimension) no expert is named by more than 4 tokens. In every micro-batch of every section some expert is named by exactly 4 tokens in every such block.
All inputs are finite; a program needn't handle non-finite values.
Results may differ from the reference program's by a relative error of at most 0.02.
Values may be sent and summed in bfloat16 or wider, within the bound.
No kernel may reach another device: no remote copies, remote signals or barrier semaphores. Data moves between devices by JAX's collectives and lax.ppermute only.
A program may use at most 128 MiB of HBM per device.

```python
import jax
import jax.numpy as jnp
from jax import lax

D = 2048
FF = 768
TOP = 4
MB = 3
TOK_MB = 64
EXPERTS = 64
TOKENS = 4096
CAP = 4
N_PIPE = 4
N_EXPERT = 64


def block_routes(block_key, busiest):
    order_key, weight_key, jitter_key, token_key = jax.random.split(block_key, 4)
    group_size = EXPERTS // TOP
    shuffle_order = jax.random.permutation(order_key, jnp.arange(EXPERTS, dtype=jnp.int32))
    leading = shuffle_order[0]
    shuffle_order = jnp.where(shuffle_order == busiest, leading, shuffle_order)
    shuffle_order = shuffle_order.at[0].set(busiest)
    chosen = shuffle_order[:group_size * TOP].reshape(TOP, group_size)
    weights = jax.random.randint(weight_key, (TOP, group_size), 0, 4)
    jitter = jax.random.randint(jitter_key, (TOP, group_size, CAP), 0, 4096)
    slot_index = jnp.arange(group_size * CAP, dtype=jnp.int32).reshape(group_size, CAP)
    scores = (weights[:, :, None] * 4096 + jitter) * 4096 + slot_index[None, :, :]
    forced = 1073741824 + slot_index[0][None, :]
    scores = scores.at[:, 0, :].set(jnp.broadcast_to(forced, (TOP, CAP)))
    flat_scores = scores.reshape(TOP, group_size * CAP).astype(jnp.int32)
    unused_values, picked = lax.top_k(flat_scores, TOK_MB)
    owner_rank = jnp.sort((picked // CAP).astype(jnp.int32), axis=1)
    column = jnp.take_along_axis(chosen, owner_rank, axis=1)
    token_keys = jax.random.split(token_key, TOP)
    orders = jax.vmap(lambda one_key: jax.random.permutation(one_key, jnp.arange(TOK_MB, dtype=jnp.int32)))(token_keys)
    shuffled = jnp.take_along_axis(column, orders.astype(jnp.int32), axis=1)
    return shuffled.T


def draw_routes(key, part):
    busy_key, blocks_key = jax.random.split(jax.random.fold_in(key, 7))
    busiest = jax.random.randint(busy_key, (N_PIPE * MB,), 0, EXPERTS).astype(jnp.int32)
    block_keys = jax.random.split(blocks_key, N_PIPE * MB * N_EXPERT)
    busiest_rep = jnp.repeat(busiest, N_EXPERT)
    blocks = jax.vmap(block_routes)(block_keys, busiest_rep)
    return blocks.reshape(N_PIPE, MB, TOKENS, TOP).astype(jnp.int32)


def block_scale(stream_key, extent, shards, smallest, largest):
    level = 1.0
    for position, blocks in shards:
        steps = jax.random.uniform(jax.random.fold_in(jax.random.fold_in(stream_key, 6), position), (blocks,), jnp.float32, smallest / len(shards), largest / len(shards))
        level = level * jnp.repeat(jnp.exp(steps), extent[position] // blocks).reshape((-1,) + (1,) * (len(extent) - 1 - position))
    return level


def centred(rng, extent, deviation, bound, cuts=(), kind=jnp.bfloat16):
    result = jax.random.normal(rng, extent, jnp.float32) * deviation
    if len(cuts) > 0:
        result = block_scale(rng, extent, cuts, -0.22, 0.18) * result
    return jnp.clip(result, min=-bound, max=bound).astype(kind)


def setup_inputs(seed: int = 0) -> dict:
    splits = jax.random.split(jax.random.key(seed), 7)
    return {
        "saved_inputs": centred(splits[0], (N_PIPE, MB, TOKENS, D), 1.0, 6.0, ((0, 4), (2, 64))),
        "routes": draw_routes(jax.random.fold_in(splits[6], 71), 0),
        "gates": jnp.clip(0.1 + 0.5 * jax.random.uniform(splits[2], (N_PIPE, MB, TOKENS, TOP), jnp.float32) ** block_scale(splits[2], (N_PIPE, MB, TOKENS, TOP), ((0, 4), (2, 64)), -0.2, 0.2), 0.1, 0.6),
        "w_in": centred(splits[3], (N_PIPE, EXPERTS, D, FF), D ** -0.5, 0.125, ((0, 4), (1, 64))),
        "w_out": centred(splits[4], (N_PIPE, EXPERTS, FF, D), FF ** -0.5, 0.21875, ((0, 4), (1, 64))),
        "cotangent": centred(splits[5], (MB, TOKENS, D), 1.0, 6.0, ((1, 64), (2, 4))),
    }


def silu_slope(preactivation):
    logistic = jax.nn.sigmoid(preactivation)
    return logistic * (1.0 + preactivation * (1.0 - logistic))


def slot_numbers(routes_micro):
    per_block = routes_micro.reshape(N_EXPERT, TOK_MB * TOP)
    expert_ids = jnp.arange(EXPERTS, dtype=jnp.int32)
    one_hot = (per_block[:, :, None] == expert_ids[None, None, :]).astype(jnp.int32)
    ranks = jnp.sum((jnp.cumsum(one_hot, axis=1) - 1) * one_hot, axis=2)
    block_ids = jnp.arange(N_EXPERT, dtype=jnp.int32)[:, None]
    slots = per_block * (N_EXPERT * CAP) + block_ids * CAP + ranks
    return slots.reshape(-1).astype(jnp.int32)


def expert_rows(operands):
    input_rows, grad_rows, first_weight, second_weight = operands
    preactivation = jnp.dot(input_rows, first_weight, preferred_element_type=jnp.float32)
    hidden_grad = jnp.dot(grad_rows, second_weight.T, preferred_element_type=jnp.float32)
    pre_grad = (hidden_grad * silu_slope(preactivation)).astype(jnp.bfloat16)
    hidden = jax.nn.silu(preactivation).astype(jnp.bfloat16)
    row_grads = jnp.dot(pre_grad, first_weight.T, preferred_element_type=jnp.float32).astype(jnp.bfloat16)
    first_grad = jnp.dot(input_rows.T, pre_grad, preferred_element_type=jnp.float32).astype(jnp.bfloat16)
    second_grad = jnp.dot(hidden.T, grad_rows, preferred_element_type=jnp.float32).astype(jnp.bfloat16)
    return row_grads, first_grad, second_grad


def section_pass(inputs_section, routes_section, gates_section, grad_section, first_weights, second_weights):
    total_slots = EXPERTS * N_EXPERT * CAP
    slot_list, input_parts, grad_parts = [], [], []
    for micro_no in range(MB):
        slots = slot_numbers(routes_section[micro_no])
        input_rep = jnp.repeat(inputs_section[micro_no], TOP, axis=0)
        gate_scaled_rows = (gates_section[micro_no][:, :, None] * grad_section[micro_no].astype(jnp.float32)[:, None, :]).astype(jnp.bfloat16)
        gate_scaled_rows = gate_scaled_rows.reshape(TOKENS * TOP, D)
        input_slots = jnp.zeros((total_slots, D), input_rep.dtype).at[slots].set(input_rep)
        gradient_slot_buffer = jnp.zeros((total_slots, D), gate_scaled_rows.dtype).at[slots].set(gate_scaled_rows)
        slot_list.append(slots)
        input_parts.append(input_slots.reshape(EXPERTS, N_EXPERT * CAP, D))
        grad_parts.append(gradient_slot_buffer.reshape(EXPERTS, N_EXPERT * CAP, D))
    input_all = jnp.concatenate(input_parts, axis=1)
    grad_all = jnp.concatenate(grad_parts, axis=1)
    row_grads, first_grad, second_grad = lax.map(expert_rows, (input_all, grad_all, first_weights, second_weights))
    span = N_EXPERT * CAP
    results = []
    for micro_no in range(MB):
        part = row_grads[:, micro_no * span:(micro_no + 1) * span, :].reshape(total_slots, D)
        returned = part[slot_list[micro_no]].astype(jnp.float32).reshape(TOKENS, TOP, D)
        grad_inputs = (grad_section[micro_no].astype(jnp.float32) + jnp.sum(returned, axis=1)).astype(jnp.bfloat16)
        results.append(grad_inputs)
    return jnp.stack(results), first_grad, second_grad


def reference(saved_inputs, routes, gates, w_in, w_out, cotangent):
    section_grad = cotangent
    firsts, seconds = [], []
    for section_no in range(N_PIPE - 1, -1, -1):
        section_grad, first_grad, second_grad = section_pass(saved_inputs[section_no], routes[section_no], gates[section_no], section_grad, w_in[section_no], w_out[section_no])
        firsts.insert(0, first_grad)
        seconds.insert(0, second_grad)
    return section_grad, jnp.stack(firsts), jnp.stack(seconds)
```

```python
import jax
import jax.numpy as jnp
from jax import lax
from jax.sharding import PartitionSpec as P


def shifted(value, axis, steps):
    count = lax.axis_size(axis)
    first, last = (max(0, -steps), min(count, count - steps))
    return lax.ppermute(value, axis, [(source, source + steps) for source in range(first, last)])


def silu_slope(preactivation):
    logistic = jax.nn.sigmoid(preactivation)
    return logistic * (1.0 + preactivation * (1.0 - logistic))


def placement_tables(routes_micro, expert_count, capacity):
    flat_routes = routes_micro.reshape(-1)
    expert_ids = jnp.arange(expert_count, dtype=jnp.int32)
    one_hot = (flat_routes[:, None] == expert_ids[None, :]).astype(jnp.int32)
    ranks = jnp.sum((jnp.cumsum(one_hot, axis=0) - 1) * one_hot, axis=1)
    slots = flat_routes * capacity + ranks
    slot_ids = jnp.arange(expert_count * capacity, dtype=jnp.int32)
    route_table = (slot_ids[:, None] == slots[None, :]).astype(jnp.bfloat16)
    slot_grid = slots.reshape(routes_micro.shape[0], routes_micro.shape[1])
    token_table = jnp.zeros((expert_count * capacity, routes_micro.shape[0]), jnp.float32)
    for route_no in range(routes_micro.shape[1]):
        token_table = token_table + (slot_ids[:, None] == slot_grid[:, route_no][None, :]).astype(
            jnp.float32
        )
    return (route_table, token_table.astype(jnp.bfloat16))


def exchange(rows):
    return lax.all_to_all(rows, "expert", split_axis=0, concat_axis=0, tiled=True)


def on_device(saved_inputs, routes, gates, w_in, w_out, cotangent):
    section_count = lax.axis_size("pipe")
    owners = lax.axis_size("expert")
    section_id = lax.axis_index("pipe")
    micro_count = saved_inputs.shape[1]
    tokens_dev = saved_inputs.shape[2]
    model_width = saved_inputs.shape[3]
    route_count = routes.shape[3]
    local_count = w_in.shape[1]
    expert_count = local_count * owners
    capacity = max(2, tokens_dev * route_count * 6 // (5 * expert_count))
    tick_count = section_count + micro_count - 1
    first_tick = section_count - 1 - section_id
    first_weights = w_in[0, 0]
    second_weights = w_out[0, 0]
    inputs_dev = saved_inputs[0]
    upstream = lax.all_gather(cotangent, "pipe", axis=2, tiled=True)
    pairs = [
        placement_tables(routes[0, micro_no], expert_count, capacity)
        for micro_no in range(micro_count)
    ]
    tables = jnp.stack([pair[0] for pair in pairs])
    token_route_tables = jnp.stack([pair[1] for pair in pairs])

    recv_inputs, slopes, hiddens = [], [], []
    for micro_no in range(micro_count):
        input_slots = jnp.dot(
            token_route_tables[micro_no], inputs_dev[micro_no], preferred_element_type=jnp.float32
        ).astype(jnp.bfloat16)
        input_recv = exchange(input_slots)
        preactivation = jnp.dot(input_recv, first_weights, preferred_element_type=jnp.float32)
        recv_inputs.append(input_recv)
        slopes.append(silu_slope(preactivation))
        hiddens.append(jax.nn.silu(preactivation).astype(jnp.bfloat16))
    recv_inputs = jnp.stack(recv_inputs)
    slopes = jnp.stack(slopes)
    hiddens = jnp.stack(hiddens)

    incoming = jnp.zeros((tokens_dev, model_width), jnp.bfloat16)
    first_acc = jnp.zeros((model_width, first_weights.shape[1]), jnp.float32)
    second_acc = jnp.zeros((second_weights.shape[0], model_width), jnp.float32)
    final_rows = []
    for tick_no in range(tick_count):
        offset = tick_no - first_tick
        valid = (offset >= 0) & (offset < micro_count)
        micro_id = jnp.clip(offset, 0, micro_count - 1)
        grad_now = jnp.where(section_id == section_count - 1, upstream[micro_id], incoming)
        gate_now = gates[0, micro_id]
        gate_scaled_rows = (gate_now[:, :, None] * grad_now.astype(jnp.float32)[:, None, :]).astype(
            jnp.bfloat16
        )
        gate_scaled_rows = gate_scaled_rows.reshape(tokens_dev * route_count, model_width)
        gradient_slot_buffer = jnp.dot(
            tables[micro_id], gate_scaled_rows, preferred_element_type=jnp.float32
        ).astype(jnp.bfloat16)
        grad_recv = exchange(gradient_slot_buffer)
        hidden_grad = lax.dot_general(
            grad_recv, second_weights, (((1,), (1,)), ((), ())), preferred_element_type=jnp.float32
        )
        pre_grad = (hidden_grad * slopes[micro_id]).astype(jnp.bfloat16)
        row_grads = lax.dot_general(
            pre_grad, first_weights, (((1,), (1,)), ((), ())), preferred_element_type=jnp.float32
        ).astype(jnp.bfloat16)
        returned = exchange(row_grads)
        summed = lax.dot_general(
            token_route_tables[micro_id],
            returned,
            (((0,), (0,)), ((), ())),
            preferred_element_type=jnp.float32,
        )
        grad_out = (grad_now.astype(jnp.float32) + summed).astype(jnp.bfloat16)
        first_term = lax.dot_general(
            recv_inputs[micro_id], pre_grad, (((0,), (0,)), ((), ())), preferred_element_type=jnp.float32
        )
        second_term = lax.dot_general(
            hiddens[micro_id], grad_recv, (((0,), (0,)), ((), ())), preferred_element_type=jnp.float32
        )
        first_acc = first_acc + jnp.where(valid, first_term, 0.0)
        second_acc = second_acc + jnp.where(valid, second_term, 0.0)
        if tick_no >= tick_count - micro_count:
            final_rows.append(grad_out)
        if tick_no + 1 < tick_count:
            incoming = shifted(grad_out, "pipe", -1)

    final_rows = jnp.stack(final_rows)
    final_term = jnp.where(section_id == 0, final_rows, jnp.zeros_like(final_rows))
    grad_in = lax.psum_scatter(final_term, "pipe", scatter_dimension=2, tiled=True)
    first_grad = first_acc.astype(jnp.bfloat16)
    second_grad = second_acc.astype(jnp.bfloat16)
    return (grad_in, first_grad[None, None], second_grad[None, None])


def solution(mesh):
    return jax.shard_map(
        on_device,
        mesh=mesh,
        in_specs=(
            P("pipe", None, "expert", None),
            P("pipe", None, "expert", None),
            P("pipe", None, "expert", None),
            P("pipe", "expert", None, None),
            P("pipe", "expert", None, None),
            P(None, "expert", "pipe"),
        ),
        out_specs=(
            P(None, "expert", "pipe"),
            P("pipe", "expert", None, None),
            P("pipe", "expert", None, None),
        ),
        check_vma=False,
    )
```

```python
import jax
import jax.numpy as jnp
from jax import lax
from jax.sharding import PartitionSpec as P


def shifted(value, axis, steps):
    count = lax.axis_size(axis)
    first, last = (max(0, -steps), min(count, count - steps))
    return lax.ppermute(value, axis, [(source, source + steps) for source in range(first, last)])


def silu_slope(preactivation):
    logistic = jax.nn.sigmoid(preactivation)
    return logistic * (1.0 + preactivation * (1.0 - logistic))


def placement_tables(routes_micro, gates_micro, owners, capacity):
    tokens, route_count = routes_micro.shape
    flat_routes = routes_micro.reshape(-1)
    expert_ids = jnp.arange(owners, dtype=jnp.int32)
    one_hot = (flat_routes[:, None] == expert_ids[None, :]).astype(jnp.int32)
    ranks = jnp.sum((jnp.cumsum(one_hot, axis=0) - 1) * one_hot, axis=1)
    slots = (flat_routes * capacity + ranks).reshape(tokens, route_count)
    slot_ids = jnp.arange(owners * capacity, dtype=jnp.int32)
    token_table = jnp.zeros((owners * capacity, tokens), jnp.float32)
    gate_table = jnp.zeros((owners * capacity, tokens), jnp.float32)
    for route_no in range(route_count):
        hit = slot_ids[:, None] == slots[:, route_no][None, :]
        token_table = token_table + hit.astype(jnp.float32)
        gate_table = gate_table + jnp.where(hit, gates_micro[:, route_no][None, :], 0.0)
    shape = (owners, capacity, tokens)
    return token_table.astype(jnp.bfloat16).reshape(shape), gate_table.reshape(shape)


def exchange(rows):
    return lax.all_to_all(rows, "expert", split_axis=0, concat_axis=0, tiled=True)


def pick(candidates, index):
    if len(candidates) == 1:
        return candidates[0]
    chosen = candidates[-1]
    for number in range(len(candidates) - 2, -1, -1):
        chosen = jnp.where(index == number, candidates[number], chosen)
    return chosen


def on_device(saved_inputs, routes, gates, w_in, w_out, cotangent):
    section_count = lax.axis_size("pipe")
    owners = lax.axis_size("expert")
    section_id = lax.axis_index("pipe")
    micro_count = saved_inputs.shape[1]
    tokens_dev = saved_inputs.shape[2]
    model_width = saved_inputs.shape[3]
    route_count = routes.shape[3]
    expert_count = w_in.shape[1] * owners
    capacity = max(2, tokens_dev * route_count * 6 // (5 * expert_count))
    tick_count = section_count + micro_count - 1
    first_tick = section_count - 1 - section_id
    first_weights = w_in[0, 0]
    second_weights = w_out[0, 0]
    inputs_dev = saved_inputs[0]
    upstream = lax.all_gather(cotangent, "pipe", axis=2, tiled=True)
    token_tables, gate_tables = [], []
    for micro_no in range(micro_count):
        token_table, gate_table = placement_tables(routes[0, micro_no], gates[0, micro_no], owners, capacity)
        token_tables.append(token_table)
        gate_tables.append(gate_table)
    token_stack = jnp.stack(token_tables)
    gate_stack = jnp.stack(gate_tables)

    recv_inputs, slopes, hiddens = [], [], []
    incoming = jnp.zeros((tokens_dev, model_width), jnp.bfloat16)
    first_acc = jnp.zeros((model_width, first_weights.shape[1]), jnp.float32)
    second_acc = jnp.zeros((second_weights.shape[0], model_width), jnp.float32)
    final_rows = []
    for tick_no in range(tick_count):
        offset = tick_no - first_tick
        valid = (offset >= 0) & (offset < micro_count)
        micro_id = jnp.clip(offset, 0, micro_count - 1)
        grad_now = jnp.where(section_id == section_count - 1, upstream[micro_id], incoming)
        gradient_slots = jnp.einsum(
            "pqk,kd->pqd",
            gate_stack[micro_id],
            grad_now.astype(jnp.float32),
            precision=lax.Precision.HIGHEST,
            preferred_element_type=jnp.float32,
        ).astype(jnp.bfloat16)
        if tick_no < micro_count:
            input_slots = jnp.einsum(
                "pqk,kd->pqd",
                token_tables[tick_no],
                inputs_dev[tick_no],
                preferred_element_type=jnp.float32,
            ).astype(jnp.bfloat16)
            both = exchange(jnp.concatenate([gradient_slots, input_slots], axis=1))
            grad_recv = both[:, :capacity]
            input_recv = both[:, capacity:]
            preactivation = jnp.einsum(
                "pqd,df->pqf", input_recv, first_weights, preferred_element_type=jnp.float32
            )
            recv_inputs.append(input_recv)
            slopes.append(silu_slope(preactivation))
            hiddens.append(jax.nn.silu(preactivation).astype(jnp.bfloat16))
        else:
            grad_recv = exchange(gradient_slots)
        hidden_grad = jnp.einsum(
            "pqd,fd->pqf", grad_recv, second_weights, preferred_element_type=jnp.float32
        )
        pre_grad = (hidden_grad * pick(slopes, micro_id)).astype(jnp.bfloat16)
        row_grads = jnp.einsum(
            "pqf,df->pqd", pre_grad, first_weights, preferred_element_type=jnp.float32
        ).astype(jnp.bfloat16)
        returned = exchange(row_grads)
        summed = jnp.einsum(
            "pqk,pqd->kd", token_stack[micro_id], returned, preferred_element_type=jnp.float32
        )
        grad_out = (grad_now.astype(jnp.float32) + summed).astype(jnp.bfloat16)
        first_term = jnp.einsum(
            "pqd,pqf->df", pick(recv_inputs, micro_id), pre_grad, preferred_element_type=jnp.float32
        )
        second_term = jnp.einsum(
            "pqf,pqd->fd", pick(hiddens, micro_id), grad_recv, preferred_element_type=jnp.float32
        )
        first_acc = first_acc + jnp.where(valid, first_term, 0.0)
        second_acc = second_acc + jnp.where(valid, second_term, 0.0)
        if tick_no >= tick_count - micro_count:
            final_rows.append(grad_out)
        if tick_no + 1 < tick_count:
            incoming = shifted(grad_out, "pipe", -1)

    final_rows = jnp.stack(final_rows)
    final_term = jnp.where(section_id == 0, final_rows, jnp.zeros_like(final_rows))
    grad_in = lax.psum_scatter(final_term, "pipe", scatter_dimension=2, tiled=True)
    first_grad = first_acc.astype(jnp.bfloat16)
    second_grad = second_acc.astype(jnp.bfloat16)
    return (grad_in, first_grad[None, None], second_grad[None, None])


def solution(mesh):
    return jax.shard_map(
        on_device,
        mesh=mesh,
        in_specs=(
            P("pipe", None, "expert", None),
            P("pipe", None, "expert", None),
            P("pipe", None, "expert", None),
            P("pipe", "expert", None, None),
            P("pipe", "expert", None, None),
            P(None, "expert", "pipe"),
        ),
        out_specs=(
            P(None, "expert", "pipe"),
            P("pipe", "expert", None, None),
            P("pipe", "expert", None, None),
        ),
        check_vma=False,
    )
```

```python
import jax
import jax.numpy as jnp
from jax import lax
from jax.sharding import PartitionSpec as P


def shifted(value, axis, steps):
    count = lax.axis_size(axis)
    first, last = (max(0, -steps), min(count, count - steps))
    return lax.ppermute(value, axis, [(source, source + steps) for source in range(first, last)])


def silu_slope(preactivation):
    logistic = jax.nn.sigmoid(preactivation)
    return logistic * (1.0 + preactivation * (1.0 - logistic))


def placement_tables(routes_micro, gates_micro, owners, capacity):
    tokens, route_count = routes_micro.shape
    flat_routes = routes_micro.reshape(-1)
    expert_ids = jnp.arange(owners, dtype=jnp.int32)
    one_hot = (flat_routes[:, None] == expert_ids[None, :]).astype(jnp.int32)
    ranks = jnp.sum((jnp.cumsum(one_hot, axis=0) - 1) * one_hot, axis=1)
    slots = (flat_routes * capacity + ranks).reshape(tokens, route_count)
    slot_ids = jnp.arange(owners * capacity, dtype=jnp.int32)
    token_table = jnp.zeros((owners * capacity, tokens), jnp.float32)
    gate_table = jnp.zeros((owners * capacity, tokens), jnp.float32)
    for route_no in range(route_count):
        hit = slot_ids[:, None] == slots[:, route_no][None, :]
        token_table = token_table + hit.astype(jnp.float32)
        gate_table = gate_table + jnp.where(hit, gates_micro[:, route_no][None, :], 0.0)
    shape = (owners, capacity, tokens)
    return token_table.astype(jnp.bfloat16).reshape(shape), gate_table.reshape(shape)


def exchange(rows):
    return lax.all_to_all(rows, "expert", split_axis=0, concat_axis=0, tiled=True)


def pick(candidates, index):
    if len(candidates) == 1:
        return candidates[0]
    chosen = candidates[-1]
    for number in range(len(candidates) - 2, -1, -1):
        chosen = jnp.where(index == number, candidates[number], chosen)
    return chosen


def on_device(saved_inputs, routes, gates, w_in, w_out, cotangent):
    section_count = lax.axis_size("pipe")
    owners = lax.axis_size("expert")
    section_id = lax.axis_index("pipe")
    micro_count = saved_inputs.shape[1]
    tokens_dev = saved_inputs.shape[2]
    model_width = saved_inputs.shape[3]
    route_count = routes.shape[3]
    expert_count = w_in.shape[1] * owners
    capacity = max(2, tokens_dev * route_count * 6 // (5 * expert_count))
    tick_count = section_count + micro_count - 1
    first_tick = section_count - 1 - section_id
    first_weights = w_in[0, 0]
    second_weights = w_out[0, 0]
    inputs_dev = saved_inputs[0]
    last_section = section_count - 1
    pieces = [
        cotangent if source == last_section else lax.ppermute(cotangent, "pipe", [(source, last_section)])
        for source in range(section_count)
    ]
    upstream = jnp.concatenate(pieces, axis=2)
    token_tables, gate_tables = [], []
    for micro_no in range(micro_count):
        token_table, gate_table = placement_tables(routes[0, micro_no], gates[0, micro_no], owners, capacity)
        token_tables.append(token_table)
        gate_tables.append(gate_table)
    token_stack = jnp.stack(token_tables)
    gate_stack = jnp.stack(gate_tables)

    recv_inputs, slopes, hiddens = [], [], []
    incoming = jnp.zeros((tokens_dev, model_width), jnp.bfloat16)
    pre_grads, grad_recvs = [], []
    final_rows = []
    for tick_no in range(tick_count):
        offset = tick_no - first_tick
        micro_id = jnp.clip(offset, 0, micro_count - 1)
        grad_now = jnp.where(section_id == section_count - 1, upstream[micro_id], incoming)
        gradient_slots = jnp.einsum(
            "pqk,kd->pqd",
            gate_stack[micro_id],
            grad_now.astype(jnp.float32),
            precision=lax.Precision.HIGHEST,
            preferred_element_type=jnp.float32,
        ).astype(jnp.bfloat16)
        if tick_no < micro_count:
            input_slots = jnp.einsum(
                "pqk,kd->pqd",
                token_tables[tick_no],
                inputs_dev[tick_no],
                preferred_element_type=jnp.float32,
            ).astype(jnp.bfloat16)
            both = exchange(jnp.concatenate([gradient_slots, input_slots], axis=1))
            grad_recv = both[:, :capacity]
            input_recv = both[:, capacity:]
            preactivation = jnp.einsum(
                "pqd,df->pqf", input_recv, first_weights, preferred_element_type=jnp.float32
            )
            recv_inputs.append(input_recv)
            slopes.append(silu_slope(preactivation))
            hiddens.append(jax.nn.silu(preactivation).astype(jnp.bfloat16))
        else:
            grad_recv = exchange(gradient_slots)
        hidden_grad = jnp.einsum(
            "pqd,fd->pqf", grad_recv, second_weights, preferred_element_type=jnp.float32
        )
        pre_grad = (hidden_grad * pick(slopes, micro_id)).astype(jnp.bfloat16)
        row_grads = jnp.einsum(
            "pqf,df->pqd", pre_grad, first_weights, preferred_element_type=jnp.float32
        ).astype(jnp.bfloat16)
        returned = exchange(row_grads)
        summed = jnp.einsum(
            "pqk,pqd->kd", token_stack[micro_id], returned, preferred_element_type=jnp.float32
        )
        grad_out = (grad_now.astype(jnp.float32) + summed).astype(jnp.bfloat16)
        pre_grads.append(pre_grad)
        grad_recvs.append(grad_recv)
        if tick_no >= tick_count - micro_count:
            final_rows.append(grad_out)
        if tick_no + 1 < tick_count:
            incoming = shifted(grad_out, "pipe", -1)

    final_rows = jnp.stack(final_rows)
    final_term = jnp.where(section_id == 0, final_rows, jnp.zeros_like(final_rows))
    grad_in = lax.psum_scatter(final_term, "pipe", scatter_dimension=2, tiled=True)
    first_terms, second_terms = [], []
    for micro_no in range(micro_count):
        own_pre = pick([pre_grads[micro_no + lag] for lag in range(section_count)], first_tick)
        own_grad = pick([grad_recvs[micro_no + lag] for lag in range(section_count)], first_tick)
        first_terms.append(jnp.einsum(
            "pqd,pqf->df", recv_inputs[micro_no], own_pre, preferred_element_type=jnp.float32
        ))
        second_terms.append(jnp.einsum(
            "pqf,pqd->fd", hiddens[micro_no], own_grad, preferred_element_type=jnp.float32
        ))
    first_grad = sum(first_terms[1:], first_terms[0]).astype(jnp.bfloat16)
    second_grad = sum(second_terms[1:], second_terms[0]).astype(jnp.bfloat16)
    return (grad_in, first_grad[None, None], second_grad[None, None])


def solution(mesh):
    return jax.shard_map(
        on_device,
        mesh=mesh,
        in_specs=(
            P("pipe", None, "expert", None),
            P("pipe", None, "expert", None),
            P("pipe", None, "expert", None),
            P("pipe", "expert", None, None),
            P("pipe", "expert", None, None),
            P(None, "expert", "pipe"),
        ),
        out_specs=(
            P(None, "expert", "pipe"),
            P("pipe", "expert", None, None),
            P("pipe", "expert", None, None),
        ),
        check_vma=False,
    )
```

```python
import jax
import jax.numpy as jnp
from jax import lax
from jax.sharding import PartitionSpec as P


def shifted(value, axis, steps):
    count = lax.axis_size(axis)
    first, last = (max(0, -steps), min(count, count - steps))
    return lax.ppermute(value, axis, [(source, source + steps) for source in range(first, last)])


def silu_slope(preactivation):
    logistic = jax.nn.sigmoid(preactivation)
    return logistic * (1.0 + preactivation * (1.0 - logistic))


def placement_tables(routes_micro, gates_micro, owners, capacity):
    tokens, route_count = routes_micro.shape
    flat_routes = routes_micro.reshape(-1)
    expert_ids = jnp.arange(owners, dtype=jnp.int32)
    one_hot = (flat_routes[:, None] == expert_ids[None, :]).astype(jnp.int32)
    ranks = jnp.sum((jnp.cumsum(one_hot, axis=0) - 1) * one_hot, axis=1)
    slots = (flat_routes * capacity + ranks).reshape(tokens, route_count)
    slot_ids = jnp.arange(owners * capacity, dtype=jnp.int32)
    token_table = jnp.zeros((owners * capacity, tokens), jnp.float32)
    gate_table = jnp.zeros((owners * capacity, tokens), jnp.float32)
    for route_no in range(route_count):
        hit = slot_ids[:, None] == slots[:, route_no][None, :]
        token_table = token_table + hit.astype(jnp.float32)
        gate_table = gate_table + jnp.where(hit, gates_micro[:, route_no][None, :], 0.0)
    shape = (owners, capacity, tokens)
    return token_table.astype(jnp.bfloat16).reshape(shape), gate_table.reshape(shape)


def exchange(rows):
    return lax.all_to_all(rows, "expert", split_axis=0, concat_axis=0, tiled=True)


def pick(candidates, index):
    if len(candidates) == 1:
        return candidates[0]
    chosen = candidates[-1]
    for number in range(len(candidates) - 2, -1, -1):
        chosen = jnp.where(index == number, candidates[number], chosen)
    return chosen


def on_device(saved_inputs, routes, gates, w_in, w_out, cotangent):
    section_count = lax.axis_size("pipe")
    owners = lax.axis_size("expert")
    section_id = lax.axis_index("pipe")
    micro_count = saved_inputs.shape[1]
    tokens_dev = saved_inputs.shape[2]
    model_width = saved_inputs.shape[3]
    route_count = routes.shape[3]
    expert_count = w_in.shape[1] * owners
    capacity = max(2, tokens_dev * route_count * 6 // (5 * expert_count))
    tick_count = section_count + micro_count - 1
    first_tick = section_count - 1 - section_id
    first_weights = w_in[0, 0]
    second_weights = w_out[0, 0]
    inputs_dev = saved_inputs[0]
    last_section = section_count - 1
    pieces = [
        cotangent if source == last_section else lax.ppermute(cotangent, "pipe", [(source, last_section)])
        for source in range(section_count)
    ]
    upstream = jnp.concatenate(pieces, axis=2)
    token_tables, gate_tables = [], []
    for micro_no in range(micro_count):
        token_table, gate_table = placement_tables(routes[0, micro_no], gates[0, micro_no], owners, capacity)
        token_tables.append(token_table)
        gate_tables.append(gate_table)
    token_stack = jnp.stack(token_tables)
    gate_stack = jnp.stack(gate_tables)

    recv_inputs, slopes, hiddens = [], [], []
    incoming = jnp.zeros((tokens_dev, model_width), jnp.bfloat16)
    pre_keep = jnp.zeros((micro_count + 1, owners, capacity, first_weights.shape[1]), jnp.bfloat16)
    grad_keep = jnp.zeros((micro_count + 1, owners, capacity, model_width), jnp.bfloat16)
    final_rows = []
    for tick_no in range(tick_count):
        offset = tick_no - first_tick
        micro_id = jnp.clip(offset, 0, micro_count - 1)
        grad_now = jnp.where(section_id == section_count - 1, upstream[micro_id], incoming)
        gradient_slots = jnp.einsum(
            "pqk,kd->pqd",
            gate_stack[micro_id],
            grad_now.astype(jnp.float32),
            precision=lax.Precision.HIGHEST,
            preferred_element_type=jnp.float32,
        ).astype(jnp.bfloat16)
        if tick_no < micro_count:
            input_slots = jnp.einsum(
                "pqk,kd->pqd",
                token_tables[tick_no],
                inputs_dev[tick_no],
                preferred_element_type=jnp.float32,
            ).astype(jnp.bfloat16)
            both = exchange(jnp.concatenate([gradient_slots, input_slots], axis=1))
            grad_recv = both[:, :capacity]
            input_recv = both[:, capacity:]
            preactivation = jnp.einsum(
                "pqd,df->pqf", input_recv, first_weights, preferred_element_type=jnp.float32
            )
            recv_inputs.append(input_recv)
            slopes.append(silu_slope(preactivation))
            hiddens.append(jax.nn.silu(preactivation).astype(jnp.bfloat16))
        else:
            grad_recv = exchange(gradient_slots)
        hidden_grad = jnp.einsum(
            "pqd,fd->pqf", grad_recv, second_weights, preferred_element_type=jnp.float32
        )
        pre_grad = (hidden_grad * pick(slopes, micro_id)).astype(jnp.bfloat16)
        row_grads = jnp.einsum(
            "pqf,df->pqd", pre_grad, first_weights, preferred_element_type=jnp.float32
        ).astype(jnp.bfloat16)
        returned = exchange(row_grads)
        summed = jnp.einsum(
            "pqk,pqd->kd", token_stack[micro_id], returned, preferred_element_type=jnp.float32
        )
        grad_out = (grad_now.astype(jnp.float32) + summed).astype(jnp.bfloat16)
        keep_at = jnp.where(offset >= micro_count, micro_count, micro_id)
        pre_keep = lax.dynamic_update_slice_in_dim(pre_keep, pre_grad[None], keep_at, 0)
        grad_keep = lax.dynamic_update_slice_in_dim(grad_keep, grad_recv[None], keep_at, 0)
        if tick_no >= tick_count - micro_count:
            final_rows.append(grad_out)
        if tick_no + 1 < tick_count:
            incoming = shifted(grad_out, "pipe", -1)

    final_rows = jnp.stack(final_rows)
    final_term = jnp.where(section_id == 0, final_rows, jnp.zeros_like(final_rows))
    grad_in = lax.psum_scatter(final_term, "pipe", scatter_dimension=2, tiled=True)
    first_grad = jnp.einsum(
        "mpqd,mpqf->df", jnp.stack(recv_inputs), pre_keep[:micro_count], preferred_element_type=jnp.float32
    ).astype(jnp.bfloat16)
    second_grad = jnp.einsum(
        "mpqf,mpqd->fd", jnp.stack(hiddens), grad_keep[:micro_count], preferred_element_type=jnp.float32
    ).astype(jnp.bfloat16)
    return (grad_in, first_grad[None, None], second_grad[None, None])


def solution(mesh):
    return jax.shard_map(
        on_device,
        mesh=mesh,
        in_specs=(
            P("pipe", None, "expert", None),
            P("pipe", None, "expert", None),
            P("pipe", None, "expert", None),
            P("pipe", "expert", None, None),
            P("pipe", "expert", None, None),
            P(None, "expert", "pipe"),
        ),
        out_specs=(
            P(None, "expert", "pipe"),
            P("pipe", "expert", None, None),
            P("pipe", "expert", None, None),
        ),
        check_vma=False,
    )
```

```python
import jax
import jax.numpy as jnp
from jax import lax
from jax.sharding import PartitionSpec as P


def shifted(value, axis, steps):
    count = lax.axis_size(axis)
    first, last = (max(0, -steps), min(count, count - steps))
    return lax.ppermute(value, axis, [(source, source + steps) for source in range(first, last)])


def silu_slope(preactivation):
    logistic = jax.nn.sigmoid(preactivation)
    return logistic * (1.0 + preactivation * (1.0 - logistic))


def placement_tables(routes_micro, gates_micro, owners, capacity):
    tokens, route_count = routes_micro.shape
    flat_routes = routes_micro.reshape(-1)
    expert_ids = jnp.arange(owners, dtype=jnp.int32)
    one_hot = (flat_routes[:, None] == expert_ids[None, :]).astype(jnp.int32)
    ranks = jnp.sum((jnp.cumsum(one_hot, axis=0) - 1) * one_hot, axis=1)
    slots = (flat_routes * capacity + ranks).reshape(tokens, route_count)
    slot_ids = jnp.arange(owners * capacity, dtype=jnp.int32)
    token_table = jnp.zeros((owners * capacity, tokens), jnp.float32)
    gate_table = jnp.zeros((owners * capacity, tokens), jnp.float32)
    for route_no in range(route_count):
        hit = slot_ids[:, None] == slots[:, route_no][None, :]
        token_table = token_table + hit.astype(jnp.float32)
        gate_table = gate_table + jnp.where(hit, gates_micro[:, route_no][None, :], 0.0)
    shape = (owners, capacity, tokens)
    return token_table.astype(jnp.bfloat16).reshape(shape), gate_table.reshape(shape)


def exchange(rows):
    return lax.all_to_all(rows, "expert", split_axis=0, concat_axis=0, tiled=True)


def pick(candidates, index):
    if len(candidates) == 1:
        return candidates[0]
    chosen = candidates[-1]
    for number in range(len(candidates) - 2, -1, -1):
        chosen = jnp.where(index == number, candidates[number], chosen)
    return chosen


def on_device(saved_inputs, routes, gates, w_in, w_out, cotangent):
    section_count = lax.axis_size("pipe")
    owners = lax.axis_size("expert")
    section_id = lax.axis_index("pipe")
    micro_count = saved_inputs.shape[1]
    tokens_dev = saved_inputs.shape[2]
    model_width = saved_inputs.shape[3]
    route_count = routes.shape[3]
    expert_count = w_in.shape[1] * owners
    capacity = max(2, tokens_dev * route_count * 6 // (5 * expert_count))
    tick_count = section_count + micro_count - 1
    first_tick = section_count - 1 - section_id
    first_weights = w_in[0, 0]
    second_weights = w_out[0, 0]
    inputs_dev = saved_inputs[0]
    last_section = section_count - 1
    pieces = [
        cotangent if source == last_section else lax.ppermute(cotangent, "pipe", [(source, last_section)])
        for source in range(section_count)
    ]
    upstream = jnp.concatenate(pieces, axis=2)
    token_tables, gate_tables = [], []
    for micro_no in range(micro_count):
        token_table, gate_table = placement_tables(routes[0, micro_no], gates[0, micro_no], owners, capacity)
        token_tables.append(token_table)
        gate_tables.append(gate_table)
    token_stack = jnp.stack(token_tables)
    gate_stack = jnp.stack(gate_tables)

    above_inputs = shifted(inputs_dev, "pipe", -1)
    above_routes = shifted(routes[0], "pipe", -1)
    above_tables = [
        placement_tables(above_routes[micro_no], gates[0, micro_no], owners, capacity)[0]
        for micro_no in range(micro_count)
    ]
    is_last = section_id == section_count - 1
    is_first = section_id == 0

    def slot_rows(table, source):
        return jnp.einsum(
            "pqk,kd->pqd",
            table,
            source,
            precision=lax.Precision.HIGHEST,
            preferred_element_type=jnp.float32,
        ).astype(jnp.bfloat16)

    recv_inputs, slopes, hiddens = [], [], []

    def add_inputs(input_recv):
        preactivation = jnp.einsum(
            "pqd,df->pqf", input_recv, first_weights, preferred_element_type=jnp.float32
        )
        recv_inputs.append(input_recv)
        slopes.append(silu_slope(preactivation))
        hiddens.append(jax.nn.silu(preactivation).astype(jnp.bfloat16))

    incoming = jnp.zeros((tokens_dev, model_width), jnp.bfloat16)
    pre_keep = jnp.zeros((micro_count + 1, owners, capacity, first_weights.shape[1]), jnp.bfloat16)
    grad_keep = jnp.zeros((micro_count + 1, owners, capacity, model_width), jnp.bfloat16)
    final_rows = []
    for tick_no in range(tick_count):
        offset = tick_no - first_tick
        micro_id = jnp.clip(offset, 0, micro_count - 1)
        grad_now = jnp.where(section_id == section_count - 1, upstream[micro_id], incoming)
        if tick_no == 0:
            first_half = slot_rows(
                jnp.where(is_last, gate_stack[micro_id], above_tables[1].astype(jnp.float32)),
                jnp.where(is_last, grad_now, above_inputs[1]).astype(jnp.float32),
            )
            own_inputs = jnp.einsum(
                "pqk,kd->pqd", token_tables[0], inputs_dev[0], preferred_element_type=jnp.float32
            ).astype(jnp.bfloat16)
            both = exchange(jnp.concatenate([first_half, own_inputs], axis=1))
            grad_recv = both[:, :capacity]
            from_below_1 = shifted(grad_recv, "pipe", 1)
            add_inputs(both[:, capacity:])
        elif tick_no == 1:
            grad_recv = exchange(slot_rows(
                jnp.where(is_first, token_tables[1].astype(jnp.float32), gate_stack[micro_id]),
                jnp.where(is_first, inputs_dev[1], grad_now).astype(jnp.float32),
            ))
            add_inputs(jnp.where(is_first, grad_recv, from_below_1))
        else:
            grad_recv = exchange(slot_rows(gate_stack[micro_id], grad_now.astype(jnp.float32)))
        hidden_grad = jnp.einsum(
            "pqd,fd->pqf", grad_recv, second_weights, preferred_element_type=jnp.float32
        )
        pre_grad = (hidden_grad * pick(slopes, micro_id)).astype(jnp.bfloat16)
        row_grads = jnp.einsum(
            "pqf,df->pqd", pre_grad, first_weights, preferred_element_type=jnp.float32
        ).astype(jnp.bfloat16)
        if tick_no == 0:
            above_second = jnp.einsum(
                "pqk,kd->pqd", above_tables[2], above_inputs[2], preferred_element_type=jnp.float32
            ).astype(jnp.bfloat16)
            returned = exchange(jnp.where(is_last, row_grads, above_second))
            from_below_2 = shifted(returned, "pipe", 1)
        elif tick_no == 1:
            own_second = jnp.einsum(
                "pqk,kd->pqd", token_tables[2], inputs_dev[2], preferred_element_type=jnp.float32
            ).astype(jnp.bfloat16)
            returned = exchange(jnp.where(is_first, own_second, row_grads))
            add_inputs(jnp.where(is_first, returned, from_below_2))
        else:
            returned = exchange(row_grads)
        summed = jnp.einsum(
            "pqk,pqd->kd", token_stack[micro_id], returned, preferred_element_type=jnp.float32
        )
        grad_out = (grad_now.astype(jnp.float32) + summed).astype(jnp.bfloat16)
        keep_at = jnp.where(offset >= micro_count, micro_count, micro_id)
        pre_keep = lax.dynamic_update_slice_in_dim(pre_keep, pre_grad[None], keep_at, 0)
        grad_keep = lax.dynamic_update_slice_in_dim(grad_keep, grad_recv[None], keep_at, 0)
        if tick_no >= tick_count - micro_count:
            final_rows.append(grad_out)
        if tick_no + 1 < tick_count:
            incoming = shifted(grad_out, "pipe", -1)

    final_rows = jnp.stack(final_rows)
    final_term = jnp.where(section_id == 0, final_rows, jnp.zeros_like(final_rows))
    grad_in = lax.psum_scatter(final_term, "pipe", scatter_dimension=2, tiled=True)
    first_grad = jnp.einsum(
        "mpqd,mpqf->df", jnp.stack(recv_inputs), pre_keep[:micro_count], preferred_element_type=jnp.float32
    ).astype(jnp.bfloat16)
    second_grad = jnp.einsum(
        "mpqf,mpqd->fd", jnp.stack(hiddens), grad_keep[:micro_count], preferred_element_type=jnp.float32
    ).astype(jnp.bfloat16)
    return (grad_in, first_grad[None, None], second_grad[None, None])


def solution(mesh):
    return jax.shard_map(
        on_device,
        mesh=mesh,
        in_specs=(
            P("pipe", None, "expert", None),
            P("pipe", None, "expert", None),
            P("pipe", None, "expert", None),
            P("pipe", "expert", None, None),
            P("pipe", "expert", None, None),
            P(None, "expert", "pipe"),
        ),
        out_specs=(
            P(None, "expert", "pipe"),
            P("pipe", "expert", None, None),
            P("pipe", "expert", None, None),
        ),
        check_vma=False,
    )
```

```python
import jax
import jax.numpy as jnp
from jax import lax
from jax.sharding import PartitionSpec as P


def shifted(value, axis, steps):
    count = lax.axis_size(axis)
    first, last = (max(0, -steps), min(count, count - steps))
    return lax.ppermute(value, axis, [(source, source + steps) for source in range(first, last)])


def silu_slope(preactivation):
    logistic = jax.nn.sigmoid(preactivation)
    return logistic * (1.0 + preactivation * (1.0 - logistic))


def placement_tables(routes_all, gates_all, owners, capacity):
    micro_count, tokens, route_count = routes_all.shape
    flat_routes = routes_all.reshape(micro_count, tokens * route_count)
    expert_ids = jnp.arange(owners, dtype=jnp.int32)
    one_hot = (flat_routes[:, :, None] == expert_ids[None, None, :]).astype(jnp.bfloat16)
    order = jnp.arange(tokens * route_count, dtype=jnp.int32)
    earlier = (order[None, :] < order[:, None]).astype(jnp.bfloat16)
    counts = jnp.einsum("ij,mje->mie", earlier, one_hot, preferred_element_type=jnp.float32)
    ranks = jnp.sum(counts * one_hot.astype(jnp.float32), axis=2).astype(jnp.int32)
    slots = (flat_routes * capacity + ranks).reshape(micro_count, tokens, route_count)
    slot_ids = jnp.arange(owners * capacity, dtype=jnp.int32)
    hit = slots[:, :, :, None] == slot_ids[None, None, None, :]
    token_table = jnp.sum(hit.astype(jnp.float32), axis=2)
    gate_table = jnp.sum(jnp.where(hit, gates_all[:, :, :, None], 0.0), axis=2)
    shape = (micro_count, owners, capacity, tokens)
    token_table = jnp.swapaxes(token_table, 1, 2).reshape(shape)
    gate_table = jnp.swapaxes(gate_table, 1, 2).reshape(shape)
    return token_table.astype(jnp.bfloat16), gate_table


def exchange(rows):
    return lax.all_to_all(rows, "expert", split_axis=0, concat_axis=0, tiled=True)


def pick(candidates, index):
    if len(candidates) == 1:
        return candidates[0]
    chosen = candidates[-1]
    for number in range(len(candidates) - 2, -1, -1):
        chosen = jnp.where(index == number, candidates[number], chosen)
    return chosen


def on_device(saved_inputs, routes, gates, w_in, w_out, cotangent):
    section_count = lax.axis_size("pipe")
    owners = lax.axis_size("expert")
    section_id = lax.axis_index("pipe")
    micro_count = saved_inputs.shape[1]
    tokens_dev = saved_inputs.shape[2]
    model_width = saved_inputs.shape[3]
    route_count = routes.shape[3]
    expert_count = w_in.shape[1] * owners
    capacity = max(2, tokens_dev * route_count * 6 // (5 * expert_count))
    tick_count = section_count + micro_count - 1
    first_tick = section_count - 1 - section_id
    first_weights = w_in[0, 0]
    second_weights = w_out[0, 0]
    inputs_dev = saved_inputs[0]
    last_section = section_count - 1
    pieces = [
        cotangent if source == last_section else lax.ppermute(cotangent, "pipe", [(source, last_section)])
        for source in range(section_count)
    ]
    upstream = jnp.concatenate(pieces, axis=2)
    token_stack, gate_stack = placement_tables(routes[0], gates[0], owners, capacity)
    token_tables = [token_stack[micro_no] for micro_no in range(micro_count)]

    above_inputs = shifted(inputs_dev, "pipe", -1)
    above_routes = shifted(routes[0], "pipe", -1)
    above_stack = placement_tables(above_routes, gates[0], owners, capacity)[0]
    above_tables = [above_stack[micro_no] for micro_no in range(micro_count)]
    is_last = section_id == section_count - 1
    is_first = section_id == 0

    def slot_rows(table, source):
        return jnp.einsum(
            "pqk,kd->pqd",
            table,
            source,
            precision=lax.Precision.HIGHEST,
            preferred_element_type=jnp.float32,
        ).astype(jnp.bfloat16)

    recv_inputs, slopes, hiddens = [], [], []

    def add_inputs(input_recv):
        preactivation = jnp.einsum(
            "pqd,df->pqf", input_recv, first_weights, preferred_element_type=jnp.float32
        )
        recv_inputs.append(input_recv)
        slopes.append(silu_slope(preactivation))
        hiddens.append(jax.nn.silu(preactivation).astype(jnp.bfloat16))

    incoming = jnp.zeros((tokens_dev, model_width), jnp.bfloat16)
    pre_keep = jnp.zeros((micro_count + 1, owners, capacity, first_weights.shape[1]), jnp.bfloat16)
    grad_keep = jnp.zeros((micro_count + 1, owners, capacity, model_width), jnp.bfloat16)
    final_rows = []
    for tick_no in range(tick_count):
        offset = tick_no - first_tick
        micro_id = jnp.clip(offset, 0, micro_count - 1)
        grad_now = jnp.where(section_id == section_count - 1, upstream[micro_id], incoming)
        if tick_no == 0:
            first_half = slot_rows(
                jnp.where(is_last, gate_stack[micro_id], above_tables[1].astype(jnp.float32)),
                jnp.where(is_last, grad_now, above_inputs[1]).astype(jnp.float32),
            )
            own_inputs = jnp.einsum(
                "pqk,kd->pqd", token_tables[0], inputs_dev[0], preferred_element_type=jnp.float32
            ).astype(jnp.bfloat16)
            both = exchange(jnp.concatenate([first_half, own_inputs], axis=1))
            grad_recv = both[:, :capacity]
            from_below_1 = shifted(grad_recv, "pipe", 1)
            add_inputs(both[:, capacity:])
        elif tick_no == 1:
            grad_recv = exchange(slot_rows(
                jnp.where(is_first, token_tables[1].astype(jnp.float32), gate_stack[micro_id]),
                jnp.where(is_first, inputs_dev[1], grad_now).astype(jnp.float32),
            ))
            add_inputs(jnp.where(is_first, grad_recv, from_below_1))
        else:
            grad_recv = exchange(slot_rows(gate_stack[micro_id], grad_now.astype(jnp.float32)))
        hidden_grad = jnp.einsum(
            "pqd,fd->pqf", grad_recv, second_weights, preferred_element_type=jnp.float32
        )
        pre_grad = (hidden_grad * pick(slopes, micro_id)).astype(jnp.bfloat16)
        row_grads = jnp.einsum(
            "pqf,df->pqd", pre_grad, first_weights, preferred_element_type=jnp.float32
        ).astype(jnp.bfloat16)
        if tick_no == 0:
            above_second = jnp.einsum(
                "pqk,kd->pqd", above_tables[2], above_inputs[2], preferred_element_type=jnp.float32
            ).astype(jnp.bfloat16)
            returned = exchange(jnp.where(is_last, row_grads, above_second))
            from_below_2 = shifted(returned, "pipe", 1)
        elif tick_no == 1:
            own_second = jnp.einsum(
                "pqk,kd->pqd", token_tables[2], inputs_dev[2], preferred_element_type=jnp.float32
            ).astype(jnp.bfloat16)
            returned = exchange(jnp.where(is_first, own_second, row_grads))
            add_inputs(jnp.where(is_first, returned, from_below_2))
        else:
            returned = exchange(row_grads)
        summed = jnp.einsum(
            "pqk,pqd->kd", token_stack[micro_id], returned, preferred_element_type=jnp.float32
        )
        grad_out = (grad_now.astype(jnp.float32) + summed).astype(jnp.bfloat16)
        keep_at = jnp.where(offset >= micro_count, micro_count, micro_id)
        pre_keep = lax.dynamic_update_slice_in_dim(pre_keep, pre_grad[None], keep_at, 0)
        grad_keep = lax.dynamic_update_slice_in_dim(grad_keep, grad_recv[None], keep_at, 0)
        if tick_no >= tick_count - micro_count:
            final_rows.append(grad_out)
        if tick_no + 1 < tick_count:
            incoming = shifted(grad_out, "pipe", -1)

    final_rows = jnp.stack(final_rows)
    final_term = jnp.where(section_id == 0, final_rows, jnp.zeros_like(final_rows))
    grad_in = lax.psum_scatter(final_term, "pipe", scatter_dimension=2, tiled=True)
    first_grad = jnp.einsum(
        "mpqd,mpqf->df", jnp.stack(recv_inputs), pre_keep[:micro_count], preferred_element_type=jnp.float32
    ).astype(jnp.bfloat16)
    second_grad = jnp.einsum(
        "mpqf,mpqd->fd", jnp.stack(hiddens), grad_keep[:micro_count], preferred_element_type=jnp.float32
    ).astype(jnp.bfloat16)
    return (grad_in, first_grad[None, None], second_grad[None, None])


def solution(mesh):
    return jax.shard_map(
        on_device,
        mesh=mesh,
        in_specs=(
            P("pipe", None, "expert", None),
            P("pipe", None, "expert", None),
            P("pipe", None, "expert", None),
            P("pipe", "expert", None, None),
            P("pipe", "expert", None, None),
            P(None, "expert", "pipe"),
        ),
        out_specs=(
            P(None, "expert", "pipe"),
            P("pipe", "expert", None, None),
            P("pipe", "expert", None, None),
        ),
        check_vma=False,
    )
```

```python
import jax
import jax.numpy as jnp
from jax import lax
from jax.sharding import PartitionSpec as P


def shifted(value, axis, steps):
    count = lax.axis_size(axis)
    first, last = (max(0, -steps), min(count, count - steps))
    return lax.ppermute(value, axis, [(source, source + steps) for source in range(first, last)])


def silu_slope(preactivation):
    logistic = jax.nn.sigmoid(preactivation)
    return logistic * (1.0 + preactivation * (1.0 - logistic))


def placement_tables(routes_all, gates_all, owners, capacity):
    micro_count, tokens, route_count = routes_all.shape
    flat_routes = routes_all.reshape(micro_count, tokens * route_count)
    expert_ids = jnp.arange(owners, dtype=jnp.int32)
    one_hot = (flat_routes[:, :, None] == expert_ids[None, None, :]).astype(jnp.bfloat16)
    order = jnp.arange(tokens * route_count, dtype=jnp.int32)
    earlier = (order[None, :] < order[:, None]).astype(jnp.bfloat16)
    counts = jnp.einsum("ij,mje->mie", earlier, one_hot, preferred_element_type=jnp.float32)
    ranks = jnp.sum(counts * one_hot.astype(jnp.float32), axis=2).astype(jnp.int32)
    slots = (flat_routes * capacity + ranks).reshape(micro_count, tokens, route_count)
    slot_ids = jnp.arange(owners * capacity, dtype=jnp.int32)
    hit = slots[:, :, :, None] == slot_ids[None, None, None, :]
    token_table = jnp.sum(hit.astype(jnp.float32), axis=2)
    gate_table = jnp.sum(jnp.where(hit, gates_all[:, :, :, None], 0.0), axis=2)
    shape = (micro_count, owners, capacity, tokens)
    token_table = jnp.swapaxes(token_table, 1, 2).reshape(shape)
    gate_table = jnp.swapaxes(gate_table, 1, 2).reshape(shape)
    return token_table.astype(jnp.bfloat16), gate_table


def exchange(rows):
    return lax.all_to_all(rows, "expert", split_axis=0, concat_axis=0, tiled=True)


def pick(candidates, index):
    if len(candidates) == 1:
        return candidates[0]
    chosen = candidates[-1]
    for number in range(len(candidates) - 2, -1, -1):
        chosen = jnp.where(index == number, candidates[number], chosen)
    return chosen


def on_device(saved_inputs, routes, gates, w_in, w_out, cotangent):
    section_count = lax.axis_size("pipe")
    owners = lax.axis_size("expert")
    section_id = lax.axis_index("pipe")
    micro_count = saved_inputs.shape[1]
    tokens_dev = saved_inputs.shape[2]
    model_width = saved_inputs.shape[3]
    route_count = routes.shape[3]
    expert_count = w_in.shape[1] * owners
    capacity = max(2, tokens_dev * route_count * 6 // (5 * expert_count))
    tick_count = section_count + micro_count - 1
    first_tick = section_count - 1 - section_id
    first_weights = w_in[0, 0]
    second_weights = w_out[0, 0]
    inputs_dev = saved_inputs[0]
    last_section = section_count - 1
    pieces = [
        cotangent if source == last_section else lax.ppermute(cotangent, "pipe", [(source, last_section)])
        for source in range(section_count)
    ]
    upstream = jnp.concatenate(pieces, axis=2)
    token_stack, gate_stack = placement_tables(routes[0], gates[0], owners, capacity)
    token_tables = [token_stack[micro_no] for micro_no in range(micro_count)]

    above_inputs = shifted(inputs_dev, "pipe", -1)
    above_routes = shifted(routes[0], "pipe", -1)
    above_stack = placement_tables(above_routes, gates[0], owners, capacity)[0]
    above_tables = [above_stack[micro_no] for micro_no in range(micro_count)]
    is_last = section_id == section_count - 1
    is_first = section_id == 0

    def slot_rows(table, source):
        return jnp.einsum(
            "pqk,kd->pqd",
            table,
            source,
            precision=lax.Precision.HIGHEST,
            preferred_element_type=jnp.float32,
        ).astype(jnp.bfloat16)

    recv_inputs, slopes, hiddens = [], [], []

    def add_inputs(input_recv):
        preactivation = jnp.einsum(
            "pqd,df->pqf", input_recv, first_weights, preferred_element_type=jnp.float32
        )
        recv_inputs.append(input_recv)
        slopes.append(silu_slope(preactivation))
        hiddens.append(jax.nn.silu(preactivation).astype(jnp.bfloat16))

    incoming = jnp.zeros((tokens_dev, model_width), jnp.bfloat16)
    pre_keep = jnp.zeros((micro_count + 1, owners, capacity, first_weights.shape[1]), jnp.bfloat16)
    grad_keep = jnp.zeros((micro_count + 1, owners, capacity, model_width), jnp.bfloat16)
    final_rows = []
    for tick_no in range(tick_count):
        offset = tick_no - first_tick
        micro_id = jnp.clip(offset, 0, micro_count - 1)
        grad_now = jnp.where(section_id == section_count - 1, upstream[micro_id], incoming)
        if tick_no == 0:
            first_half = slot_rows(
                jnp.where(is_last, gate_stack[micro_id], above_tables[1].astype(jnp.float32)),
                jnp.where(is_last, grad_now, above_inputs[1]).astype(jnp.float32),
            )
            own_inputs = jnp.einsum(
                "pqk,kd->pqd", token_tables[0], inputs_dev[0], preferred_element_type=jnp.float32
            ).astype(jnp.bfloat16)
            both = exchange(jnp.concatenate([first_half, own_inputs], axis=1))
            grad_recv = both[:, :capacity]
            from_below_1 = shifted(grad_recv, "pipe", 1)
            add_inputs(both[:, capacity:])
        elif tick_no == 1:
            grad_recv = exchange(slot_rows(
                jnp.where(is_first, token_tables[1].astype(jnp.float32), gate_stack[micro_id]),
                jnp.where(is_first, inputs_dev[1], grad_now).astype(jnp.float32),
            ))
            add_inputs(jnp.where(is_first, grad_recv, from_below_1))
        else:
            grad_recv = exchange(slot_rows(gate_stack[micro_id], grad_now.astype(jnp.float32)))
        hidden_grad = jnp.einsum(
            "pqd,fd->pqf", grad_recv, second_weights, preferred_element_type=jnp.float32
        )
        pre_grad = (hidden_grad * pick(slopes, micro_id)).astype(jnp.bfloat16)
        row_grads = jnp.einsum(
            "pqf,df->pqd", pre_grad, first_weights, preferred_element_type=jnp.float32
        ).astype(jnp.bfloat16)
        if tick_no == 0:
            above_second = jnp.einsum(
                "pqk,kd->pqd", above_tables[2], above_inputs[2], preferred_element_type=jnp.float32
            ).astype(jnp.bfloat16)
            returned = exchange(jnp.where(is_last, row_grads, above_second))
            from_below_2 = shifted(returned, "pipe", 1)
        elif tick_no == 1:
            own_second = jnp.einsum(
                "pqk,kd->pqd", token_tables[2], inputs_dev[2], preferred_element_type=jnp.float32
            ).astype(jnp.bfloat16)
            returned = exchange(jnp.where(is_first, own_second, row_grads))
            add_inputs(jnp.where(is_first, returned, from_below_2))
        else:
            returned = exchange(row_grads)
        if tick_no == tick_count - 1:
            keep_at = jnp.where(offset >= micro_count, micro_count, micro_id)
            pre_keep = lax.dynamic_update_slice_in_dim(pre_keep, pre_grad[None], keep_at, 0)
            grad_keep = lax.dynamic_update_slice_in_dim(grad_keep, grad_recv[None], keep_at, 0)
            first_sum = jnp.einsum(
                "mpqd,mpqf->df", jnp.stack(recv_inputs), pre_keep[:micro_count],
                preferred_element_type=jnp.float32,
            )
            second_sum = jnp.einsum(
                "mpqf,mpqd->fd", jnp.stack(hiddens), grad_keep[:micro_count],
                preferred_element_type=jnp.float32,
            )
            returned, first_sum, second_sum = lax.optimization_barrier((returned, first_sum, second_sum))
        summed = jnp.einsum(
            "pqk,pqd->kd", token_stack[micro_id], returned, preferred_element_type=jnp.float32
        )
        grad_out = (grad_now.astype(jnp.float32) + summed).astype(jnp.bfloat16)
        if tick_no < tick_count - 1:
            keep_at = jnp.where(offset >= micro_count, micro_count, micro_id)
            pre_keep = lax.dynamic_update_slice_in_dim(pre_keep, pre_grad[None], keep_at, 0)
            grad_keep = lax.dynamic_update_slice_in_dim(grad_keep, grad_recv[None], keep_at, 0)
        if tick_no >= tick_count - micro_count:
            final_rows.append(grad_out)
        if tick_no + 1 < tick_count:
            incoming = shifted(grad_out, "pipe", -1)

    final_rows = jnp.stack(final_rows)
    final_term = jnp.where(section_id == 0, final_rows, jnp.zeros_like(final_rows))
    grad_in = lax.psum_scatter(final_term, "pipe", scatter_dimension=2, tiled=True)
    first_grad = first_sum.astype(jnp.bfloat16)
    second_grad = second_sum.astype(jnp.bfloat16)
    return (grad_in, first_grad[None, None], second_grad[None, None])


def solution(mesh):
    return jax.shard_map(
        on_device,
        mesh=mesh,
        in_specs=(
            P("pipe", None, "expert", None),
            P("pipe", None, "expert", None),
            P("pipe", None, "expert", None),
            P("pipe", "expert", None, None),
            P("pipe", "expert", None, None),
            P(None, "expert", "pipe"),
        ),
        out_specs=(
            P(None, "expert", "pipe"),
            P("pipe", "expert", None, None),
            P("pipe", "expert", None, None),
        ),
        check_vma=False,
    )
```

```python
import jax
import jax.numpy as jnp
from jax import lax
from jax.sharding import PartitionSpec as P


def shifted(value, axis, steps):
    count = lax.axis_size(axis)
    first, last = (max(0, -steps), min(count, count - steps))
    return lax.ppermute(value, axis, [(source, source + steps) for source in range(first, last)])


def silu_slope(preactivation):
    logistic = jax.nn.sigmoid(preactivation)
    return logistic * (1.0 + preactivation * (1.0 - logistic))


def placement_tables(routes_all, gates_all, owners, capacity):
    micro_count, tokens, route_count = routes_all.shape
    flat_routes = routes_all.reshape(micro_count, tokens * route_count)
    expert_ids = jnp.arange(owners, dtype=jnp.int32)
    one_hot = (flat_routes[:, :, None] == expert_ids[None, None, :]).astype(jnp.bfloat16)
    order = jnp.arange(tokens * route_count, dtype=jnp.int32)
    earlier = (order[None, :] < order[:, None]).astype(jnp.bfloat16)
    counts = jnp.einsum("ij,mje->mie", earlier, one_hot, preferred_element_type=jnp.float32)
    ranks = jnp.sum(counts * one_hot.astype(jnp.float32), axis=2).astype(jnp.int32)
    slots = (flat_routes * capacity + ranks).reshape(micro_count, tokens, route_count)
    slot_ids = jnp.arange(owners * capacity, dtype=jnp.int32)
    hit = slots[:, :, :, None] == slot_ids[None, None, None, :]
    token_table = jnp.sum(hit.astype(jnp.float32), axis=2)
    gate_table = jnp.sum(jnp.where(hit, gates_all[:, :, :, None], 0.0), axis=2)
    shape = (micro_count, owners, capacity, tokens)
    token_table = jnp.swapaxes(token_table, 1, 2).reshape(shape)
    gate_table = jnp.swapaxes(gate_table, 1, 2).reshape(shape)
    return token_table.astype(jnp.bfloat16), gate_table


def exchange(rows):
    return lax.all_to_all(rows, "expert", split_axis=0, concat_axis=0, tiled=True)


def pick(candidates, index):
    if len(candidates) == 1:
        return candidates[0]
    chosen = candidates[-1]
    for number in range(len(candidates) - 2, -1, -1):
        chosen = jnp.where(index == number, candidates[number], chosen)
    return chosen


def on_device(saved_inputs, routes, gates, w_in, w_out, cotangent):
    section_count = lax.axis_size("pipe")
    owners = lax.axis_size("expert")
    section_id = lax.axis_index("pipe")
    micro_count = saved_inputs.shape[1]
    tokens_dev = saved_inputs.shape[2]
    model_width = saved_inputs.shape[3]
    route_count = routes.shape[3]
    expert_count = w_in.shape[1] * owners
    capacity = max(2, tokens_dev * route_count * 6 // (5 * expert_count))
    tick_count = section_count + micro_count - 1
    first_tick = section_count - 1 - section_id
    first_weights = w_in[0, 0]
    second_weights = w_out[0, 0]
    inputs_dev = saved_inputs[0]
    last_section = section_count - 1
    pieces = [
        cotangent if source == last_section else lax.ppermute(cotangent, "pipe", [(source, last_section)])
        for source in range(section_count)
    ]
    upstream = jnp.concatenate(pieces, axis=2)
    token_stack, gate_stack = placement_tables(routes[0], gates[0], owners, capacity)
    token_tables = [token_stack[micro_no] for micro_no in range(micro_count)]

    above_inputs = shifted(inputs_dev, "pipe", -1)
    above_routes = shifted(routes[0], "pipe", -1)
    above_stack = placement_tables(above_routes, gates[0], owners, capacity)[0]
    above_tables = [above_stack[micro_no] for micro_no in range(micro_count)]
    is_last = section_id == section_count - 1
    is_first = section_id == 0

    def slot_rows(table, source):
        return jnp.einsum(
            "pqk,kd->pqd",
            table,
            source,
            precision=lax.Precision.HIGHEST,
            preferred_element_type=jnp.float32,
        ).astype(jnp.bfloat16)

    recv_inputs, slopes, hiddens = [], [], []

    def add_inputs(input_recv):
        preactivation = jnp.einsum(
            "pqd,df->pqf", input_recv, first_weights, preferred_element_type=jnp.float32
        )
        recv_inputs.append(input_recv)
        slopes.append(silu_slope(preactivation))
        hiddens.append(jax.nn.silu(preactivation).astype(jnp.bfloat16))

    incoming = jnp.zeros((tokens_dev, model_width), jnp.bfloat16)
    pre_keep = jnp.zeros((micro_count + 1, owners, capacity, first_weights.shape[1]), jnp.bfloat16)
    grad_keep = jnp.zeros((micro_count + 1, owners, capacity, model_width), jnp.bfloat16)
    final_rows = []
    for tick_no in range(tick_count):
        offset = tick_no - first_tick
        micro_id = jnp.clip(offset, 0, micro_count - 1)
        grad_now = jnp.where(section_id == section_count - 1, upstream[micro_id], incoming)
        if tick_no == 0:
            first_half = slot_rows(
                jnp.where(is_last, gate_stack[micro_id], above_tables[1].astype(jnp.float32)),
                jnp.where(is_last, grad_now, above_inputs[1]).astype(jnp.float32),
            )
            own_inputs = jnp.einsum(
                "pqk,kd->pqd", token_tables[0], inputs_dev[0], preferred_element_type=jnp.float32
            ).astype(jnp.bfloat16)
            both = exchange(jnp.concatenate([first_half, own_inputs], axis=1))
            grad_recv = both[:, :capacity]
            from_below_1 = shifted(grad_recv, "pipe", 1)
            add_inputs(both[:, capacity:])
        elif tick_no == 1:
            grad_recv = exchange(slot_rows(
                jnp.where(is_first, token_tables[1].astype(jnp.float32), gate_stack[micro_id]),
                jnp.where(is_first, inputs_dev[1], grad_now).astype(jnp.float32),
            ))
            add_inputs(jnp.where(is_first, grad_recv, from_below_1))
        else:
            grad_recv = exchange(slot_rows(gate_stack[micro_id], grad_now.astype(jnp.float32)))
        hidden_grad = jnp.einsum(
            "pqd,fd->pqf", grad_recv, second_weights, preferred_element_type=jnp.float32
        )
        pre_grad = (hidden_grad * pick(slopes, micro_id)).astype(jnp.bfloat16)
        row_grads = jnp.einsum(
            "pqf,df->pqd", pre_grad, first_weights, preferred_element_type=jnp.float32
        ).astype(jnp.bfloat16)
        if tick_no == 0:
            above_second = jnp.einsum(
                "pqk,kd->pqd", above_tables[2], above_inputs[2], preferred_element_type=jnp.float32
            ).astype(jnp.bfloat16)
            returned = exchange(jnp.where(is_last, row_grads, above_second))
            from_below_2 = shifted(returned, "pipe", 1)
        elif tick_no == 1:
            own_second = jnp.einsum(
                "pqk,kd->pqd", token_tables[2], inputs_dev[2], preferred_element_type=jnp.float32
            ).astype(jnp.bfloat16)
            returned = exchange(jnp.where(is_first, own_second, row_grads))
            add_inputs(jnp.where(is_first, returned, from_below_2))
        else:
            returned = exchange(row_grads)
        if tick_no == tick_count - 1:
            keep_at = jnp.where(offset >= micro_count, micro_count, micro_id)
            pre_keep = lax.dynamic_update_slice_in_dim(pre_keep, pre_grad[None], keep_at, 0)
            grad_keep = lax.dynamic_update_slice_in_dim(grad_keep, grad_recv[None], keep_at, 0)
            first_sum = jnp.einsum(
                "mpqd,mpqf->df", jnp.stack(recv_inputs), pre_keep[:micro_count],
                preferred_element_type=jnp.float32,
            )
            second_sum = jnp.einsum(
                "mpqf,mpqd->fd", jnp.stack(hiddens), grad_keep[:micro_count],
                preferred_element_type=jnp.float32,
            )
            returned, first_sum, second_sum = lax.optimization_barrier((returned, first_sum, second_sum))
        summed = jnp.einsum(
            "pqk,pqd->kd", token_stack[micro_id], returned, preferred_element_type=jnp.float32
        )
        grad_out = (grad_now.astype(jnp.float32) + summed).astype(jnp.bfloat16)
        if tick_no < tick_count - 1:
            keep_at = jnp.where(offset >= micro_count, micro_count, micro_id)
            pre_keep = lax.dynamic_update_slice_in_dim(pre_keep, pre_grad[None], keep_at, 0)
            grad_keep = lax.dynamic_update_slice_in_dim(grad_keep, grad_recv[None], keep_at, 0)
        if tick_no >= tick_count - micro_count:
            width_part = model_width // section_count
            parts = [grad_out[:, number * width_part:(number + 1) * width_part] for number in range(section_count)]
            landed = parts[0]
            for number in range(1, section_count):
                moved = lax.ppermute(parts[number], "pipe", [(0, number)])
                landed = jnp.where(section_id == number, moved, landed)
            final_rows.append(landed)
        if tick_no + 1 < tick_count:
            incoming = shifted(grad_out, "pipe", -1)

    grad_in = jnp.stack(final_rows)
    first_grad = first_sum.astype(jnp.bfloat16)
    second_grad = second_sum.astype(jnp.bfloat16)
    return (grad_in, first_grad[None, None], second_grad[None, None])


def solution(mesh):
    return jax.shard_map(
        on_device,
        mesh=mesh,
        in_specs=(
            P("pipe", None, "expert", None),
            P("pipe", None, "expert", None),
            P("pipe", None, "expert", None),
            P("pipe", "expert", None, None),
            P("pipe", "expert", None, None),
            P(None, "expert", "pipe"),
        ),
        out_specs=(
            P(None, "expert", "pipe"),
            P("pipe", "expert", None, None),
            P("pipe", "expert", None, None),
        ),
        check_vma=False,
    )
```
